1024 devices in a mesh: tile: 32 (over z, x_hi), kern: 32 (over y, x_lo, core).
Axes of the slice: x: 4 (x_hi: 2, x_lo: 2; x = x_hi * 2 + x_lo), y: 8, z: 16, core: 2. Of those that a mesh axis runs over, the one named last changes fastest.
Arguments:
- mask: float32 [64, 4096], P(None, 'tile'), may hold values from 0 to 1
- kernels: float32 [32, 2, 129, 129], P('kern'), may hold values from -0.046875 to 0.046875
- weights: float32 [32], P('kern'), may hold values from 0.3 to 3
- target: int32 [64, 4096], P(None, 'tile'), may hold values 0 or 1
- active: int32 [2, 128], P(None, 'tile'), may hold values 0 or 1
Outputs:
- mask_grad: float32 [64, 4096], P(None, 'tile')
The draws below stay inside these ranges and needn't reach their ends.
All inputs are finite; a program needn't handle non-finite values. No bound on the sum of `target` or of `active` on one device may be relied on, other than what follows from the above.
Results may differ from the reference program's by a relative error of at most 0.0001.
Values sent between devices are 32-bit elements; how exact they have to be, the bound alone decides.
No kernel may reach another device: no remote copies, remote signals or barrier semaphores. Data moves between devices by JAX's collectives and lax.ppermute only.
A program may use at most 32 MiB of HBM per device.

```python
import math
import jax
import jax.numpy as jnp
from jax import lax

BAND = 64
KS = 129
BLK = 32
KERNELS = 32
NCOLS = 4096


def with_ends(values, key, smallest, top_value):
    place = [jax.random.randint(jax.random.fold_in(key, axis), (), 0, length) for axis, length in enumerate(values.shape)]
    widest = values.shape.index(max(values.shape))
    beside = place[:widest] + [(place[widest] + 1) % values.shape[widest]] + place[widest + 1:]
    return values.at[tuple(place)].set(smallest).at[tuple(beside)].set(top_value)


def level_of(rng, dims, shards, least, largest):
    level = 1.0
    for position, shards_of in shards:
        heights = jax.random.uniform(jax.random.fold_in(jax.random.fold_in(rng, 6), position), (shards_of,), jnp.float32, least / len(shards), largest / len(shards))
        level = level * jnp.repeat(jnp.exp(heights), dims[position] // shards_of).reshape((-1,) + (1,) * (len(dims) - 1 - position))
    return level


def gaussian(key, extent, scale, limit, cuts=(), held_as=jnp.bfloat16):
    values = jax.random.normal(key, extent, jnp.float32) * scale
    if len(cuts) > 0:
        values = level_of(key, extent, cuts, -0.22, 0.18) * values
    return jnp.clip(values, min=-limit, max=limit).astype(held_as)


def setup_inputs(seed: int = 0) -> dict:
    seeds = jax.random.split(jax.random.key(seed), 6)
    return {
        "mask": jnp.clip(1.0 * jax.random.uniform(seeds[0], (BAND, NCOLS), jnp.float32) ** level_of(seeds[0], (BAND, NCOLS), ((1, 32),), -0.2, 0.2), 0.0, 1.0),
        "kernels": gaussian(seeds[1], (KERNELS, 2, KS, KS), (KS * KS) ** -0.5, 0.046875, ((0, 32),), jnp.float32),
        "weights": jnp.clip(jnp.exp(math.log(3.0) - 2.3025851 * jax.random.uniform(seeds[2], (KERNELS,), jnp.float32) ** level_of(seeds[2], (KERNELS,), ((0, 32),), -0.2, 0.2)), 0.3, 3.0),
        "target": with_ends((jax.random.randint(seeds[3], (BAND, NCOLS), 0, 2) < 1).astype(jnp.int32), jax.random.fold_in(seeds[3], 1), 0, 1),
        "active": with_ends((jax.random.randint(seeds[4], (BAND // BLK, NCOLS // BLK), 0, 4) < 3).astype(jnp.int32), jax.random.fold_in(seeds[4], 1), 0, 1),
    }


STEEPNESS = 6.0
THRESHOLD = 0.8


def reference(mask, kernels, weights, target, active):
    margin = (KS - 1) // 2
    padded = jnp.pad(mask, margin)
    full_rows = BAND + 4 * margin
    full_cols = NCOLS + 4 * margin
    padded_spec = jnp.fft.fft2(padded, s=(full_rows, full_cols))

    def forward(kernel):
        complex_kernel = kernel[0] + 1j * kernel[1]
        flipped = complex_kernel[::-1, ::-1]
        convolved = jnp.fft.ifft2(padded_spec * jnp.fft.fft2(flipped, s=(full_rows, full_cols)))
        window = convolved[2 * margin:2 * margin + BAND, 2 * margin:2 * margin + NCOLS]
        return jnp.stack([jnp.real(window), jnp.imag(window)]).astype(mask.dtype)

    fields = lax.map(forward, kernels)
    intensity = jnp.sum(weights[:, None, None] * (fields[:, 0] ** 2 + fields[:, 1] ** 2), axis=0) / KERNELS
    resist = jax.nn.sigmoid(STEEPNESS * (intensity - THRESHOLD))
    pixel_active = jnp.repeat(jnp.repeat(active, BLK, axis=0), BLK, axis=1).astype(mask.dtype)
    drive = 2.0 * (resist - target.astype(mask.dtype)) * pixel_active * STEEPNESS * resist * (1.0 - resist)

    def adjoint(total, item):
        kernel, field, weight = item
        conj_kernel = kernel[0] - 1j * kernel[1]
        source = drive * field[0] + 1j * (drive * field[1])
        rows_out = BAND + 2 * margin
        cols_out = NCOLS + 2 * margin
        convolved = jnp.fft.ifft2(jnp.fft.fft2(source, s=(rows_out, cols_out)) * jnp.fft.fft2(conj_kernel, s=(rows_out, cols_out)))
        back = jnp.real(convolved)[margin:margin + BAND, margin:margin + NCOLS].astype(mask.dtype)
        return total + (2.0 * weight / KERNELS) * back, None

    mask_grad, unused = lax.scan(adjoint, jnp.zeros((BAND, NCOLS), mask.dtype), (kernels, fields, weights))
    return mask_grad
```

```python
import math

import jax
import jax.numpy as jnp
from jax import lax
from jax.sharding import PartitionSpec as P

BLK = 32


STEEPNESS = 6.0
THRESHOLD = 0.8


def padded(shard, sides, width):
    for axis, dim in sides:
        peers, length = (lax.axis_size(axis), shard.shape[dim])
        up = [(i, (i + 1) % peers) for i in range(peers - 1)]
        down = [(j, i) for i, j in up]
        last = lax.slice_in_dim(shard, length - width, length, axis=dim)
        initial = lax.slice_in_dim(shard, 0, width, axis=dim)
        before = lax.ppermute(last, axis, up)
        after = lax.ppermute(initial, axis, down)
        shard = jnp.concatenate([before, shard, after], axis=dim)
    return shard


def exchange_sum(value, axis):
    peers = lax.axis_size(axis)
    if peers & (peers - 1):
        return lax.psum(value, axis)
    stride = 1
    while stride < peers:
        pairs = [(i, i ^ stride) for i in range(peers)]
        value = value + lax.ppermute(value, axis, pairs)
        stride *= 2
    return value


def product(left_mat, right_mat):
    return jnp.dot(
        left_mat, right_mat, precision=lax.Precision.HIGHEST, preferred_element_type=jnp.float32
    )


def twiddle(length):
    series = jnp.arange(length, dtype=jnp.int32)
    phase = series[:, None] * series[None, :] % length
    angle = phase.astype(jnp.float32) * (2.0 * math.pi / length)
    return (jnp.cos(angle), jnp.sin(angle))


def apply_left(cosine, sine, sign, real_part, imag_part):
    return (
        product(cosine, real_part) - sign * product(sine, imag_part),
        product(cosine, imag_part) + sign * product(sine, real_part),
    )


def apply_right(real_part, imag_part, cosine, sine, sign):
    return (
        product(real_part, cosine) - sign * product(imag_part, sine),
        product(imag_part, cosine) + sign * product(real_part, sine),
    )


def edge_pixels(frame, margin):
    return jnp.concatenate([frame[:, :margin], frame[:, frame.shape[1] - margin :]], axis=1)


def add_returned(own, returned, margin):
    from_left = returned[:, :margin]
    from_right = returned[:, returned.shape[1] - margin :]
    own = own.at[:, :margin].add(from_left)
    return own.at[:, own.shape[1] - margin :].add(from_right)


def resist_drive(intensity, target_rows, active_rows):
    resist = jax.nn.sigmoid(STEEPNESS * (intensity - THRESHOLD))
    return 2.0 * (resist - target_rows) * active_rows * STEEPNESS * resist * (1.0 - resist)


def body(mask, kernels, weights, target, active):
    band, own_cols = mask.shape
    width = kernels.shape[-1]
    margin = (width - 1) // 2
    frame_rows = band + 2 * margin
    frame_cols = own_cols + 2 * margin
    total_kernels = kernels.shape[0] * lax.axis_size("kern")
    scale = 1.0 / (frame_rows * frame_cols)
    row_cos, row_sin = twiddle(frame_rows)
    col_cos, col_sin = twiddle(frame_cols)
    extended = padded(mask, (("tile", 1),), margin)
    spec_real = product(row_cos[:, margin : margin + band], extended)
    spec_imag = -product(row_sin[:, margin : margin + band], extended)
    spec_real, spec_imag = apply_right(spec_real, spec_imag, col_cos, col_sin, -1.0)
    kernel_index = 0
    kern_real, kern_imag = apply_left(
        row_cos[:, :width],
        row_sin[:, :width],
        1.0,
        kernels[kernel_index, 0],
        kernels[kernel_index, 1],
    )
    kern_real, kern_imag = apply_right(
        kern_real, kern_imag, col_cos[:width, :], col_sin[:width, :], 1.0
    )
    prod_real = spec_real * kern_real - spec_imag * kern_imag
    prod_imag = spec_real * kern_imag + spec_imag * kern_real
    field_real, field_imag = apply_left(
        row_cos[:band, :], row_sin[:band, :], 1.0, prod_real, prod_imag
    )
    field_real, field_imag = apply_right(
        field_real, field_imag, col_cos[:, :own_cols], col_sin[:, :own_cols], 1.0
    )
    field_real = field_real * scale
    field_imag = field_imag * scale
    responses = [(kern_real, kern_imag, field_real, field_imag)]
    share_sum = weights[kernel_index] * (field_real * field_real + field_imag * field_imag)
    share_sum = share_sum / total_kernels
    target_float = target.astype(jnp.float32)
    pixel_active = jnp.repeat(jnp.repeat(active, BLK, axis=0), BLK, axis=1).astype(jnp.float32)
    intensity = exchange_sum(share_sum, "kern")
    drive = resist_drive(intensity, target_float, pixel_active)
    kernel_index = 0
    kern_real, kern_imag, field_real, field_imag = responses[kernel_index]
    source_real, source_imag = apply_left(
        row_cos[:, :band], row_sin[:, :band], -1.0, drive * field_real, drive * field_imag
    )
    source_real, source_imag = apply_right(
        source_real, source_imag, col_cos[:own_cols, :], col_sin[:own_cols, :], -1.0
    )
    quot_real = source_real * kern_real + source_imag * kern_imag
    quot_imag = source_imag * kern_real - source_real * kern_imag
    back_real, back_imag = apply_left(
        row_cos[margin : margin + band, :],
        row_sin[margin : margin + band, :],
        1.0,
        quot_real,
        quot_imag,
    )
    back = product(back_real, col_cos) - product(back_imag, col_sin)
    frame_grad = 2.0 * weights[kernel_index] * scale / total_kernels * back
    summed = exchange_sum(frame_grad, "kern")
    returned = padded(edge_pixels(summed, margin), (("tile", 1),), margin)
    mask_grad = add_returned(summed[:, margin : margin + own_cols], returned, margin)
    return mask_grad


def solution(mesh):
    return jax.shard_map(
        body,
        mesh=mesh,
        in_specs=(
            P(None, "tile"),
            P("kern", None, None, None),
            P("kern"),
            P(None, "tile"),
            P(None, "tile"),
        ),
        out_specs=P(None, "tile"),
        check_vma=False,
    )
```

```python
import math

import jax
import jax.numpy as jnp
from jax import lax
from jax.sharding import PartitionSpec as P

BLK = 32


STEEPNESS = 6.0
THRESHOLD = 0.8


def padded(shard, sides, width):
    for axis, dim in sides:
        peers, length = (lax.axis_size(axis), shard.shape[dim])
        up = [(i, (i + 1) % peers) for i in range(peers - 1)]
        down = [(j, i) for i, j in up]
        last = lax.slice_in_dim(shard, length - width, length, axis=dim)
        initial = lax.slice_in_dim(shard, 0, width, axis=dim)
        before = lax.ppermute(last, axis, up)
        after = lax.ppermute(initial, axis, down)
        shard = jnp.concatenate([before, shard, after], axis=dim)
    return shard


def exchange_sum(value, axis):
    peers = lax.axis_size(axis)
    if peers & (peers - 1):
        return lax.psum(value, axis)
    stride = 1
    while stride < peers:
        pairs = [(i, i ^ stride) for i in range(peers)]
        value = value + lax.ppermute(value, axis, pairs)
        stride *= 2
    return value


def product(left_mat, right_mat):
    return jnp.dot(
        left_mat, right_mat, precision=lax.Precision.HIGHEST, preferred_element_type=jnp.float32
    )


def twiddle(length):
    series = jnp.arange(length, dtype=jnp.int32)
    phase = series[:, None] * series[None, :] % length
    angle = phase.astype(jnp.float32) * (2.0 * math.pi / length)
    return (jnp.cos(angle), jnp.sin(angle))


def apply_left(cosine, sine, sign, real_part, imag_part):
    return (
        product(cosine, real_part) - sign * product(sine, imag_part),
        product(cosine, imag_part) + sign * product(sine, real_part),
    )


def apply_right(real_part, imag_part, cosine, sine, sign):
    return (
        product(real_part, cosine) - sign * product(imag_part, sine),
        product(imag_part, cosine) + sign * product(real_part, sine),
    )


def edge_pixels(frame, margin):
    return jnp.concatenate([frame[:, :margin], frame[:, frame.shape[1] - margin :]], axis=1)


def add_returned(own, returned, margin):
    from_left = returned[:, :margin]
    from_right = returned[:, returned.shape[1] - margin :]
    own = own.at[:, :margin].add(from_left)
    return own.at[:, own.shape[1] - margin :].add(from_right)


def resist_drive(intensity, target_rows, active_rows):
    resist = jax.nn.sigmoid(STEEPNESS * (intensity - THRESHOLD))
    return 2.0 * (resist - target_rows) * active_rows * STEEPNESS * resist * (1.0 - resist)


def body(mask, kernels, weights, target, active):
    band, own_cols = mask.shape
    width = kernels.shape[-1]
    margin = (width - 1) // 2
    frame_rows = band + 2 * margin
    frame_cols = own_cols + 2 * margin
    total_kernels = kernels.shape[0] * lax.axis_size("kern")
    scale = 1.0 / (frame_rows * frame_cols)
    row_cos, row_sin = twiddle(frame_rows)
    col_cos, col_sin = twiddle(frame_cols)
    extended = padded(mask, (("tile", 1),), margin)
    cols_real = product(extended, col_cos)
    cols_imag = -product(extended, col_sin)
    spec_real, spec_imag = apply_left(
        row_cos[:, margin : margin + band],
        row_sin[:, margin : margin + band],
        -1.0,
        cols_real,
        cols_imag,
    )
    kernel_index = 0
    kern_real, kern_imag = apply_left(
        row_cos[:, :width],
        row_sin[:, :width],
        1.0,
        kernels[kernel_index, 0],
        kernels[kernel_index, 1],
    )
    kern_real, kern_imag = apply_right(
        kern_real, kern_imag, col_cos[:width, :], col_sin[:width, :], 1.0
    )
    prod_real = spec_real * kern_real - spec_imag * kern_imag
    prod_imag = spec_real * kern_imag + spec_imag * kern_real
    field_real, field_imag = apply_left(
        row_cos[:band, :], row_sin[:band, :], 1.0, prod_real, prod_imag
    )
    field_real, field_imag = apply_right(
        field_real, field_imag, col_cos[:, :own_cols], col_sin[:, :own_cols], 1.0
    )
    field_real = field_real * scale
    field_imag = field_imag * scale
    responses = [(kern_real, kern_imag, field_real, field_imag)]
    share_sum = weights[kernel_index] * (field_real * field_real + field_imag * field_imag)
    share_sum = share_sum / total_kernels
    target_float = target.astype(jnp.float32)
    pixel_active = jnp.repeat(jnp.repeat(active, BLK, axis=0), BLK, axis=1).astype(jnp.float32)
    intensity = exchange_sum(share_sum, "kern")
    drive = resist_drive(intensity, target_float, pixel_active)
    kernel_index = 0
    kern_real, kern_imag, field_real, field_imag = responses[kernel_index]
    source_real, source_imag = apply_right(
        drive * field_real, drive * field_imag, col_cos[:own_cols, :], col_sin[:own_cols, :], -1.0
    )
    source_real, source_imag = apply_left(
        row_cos[:, :band], row_sin[:, :band], -1.0, source_real, source_imag
    )
    quot_real = source_real * kern_real + source_imag * kern_imag
    quot_imag = source_imag * kern_real - source_real * kern_imag
    back_real, back_imag = apply_left(
        row_cos[margin : margin + band, :],
        row_sin[margin : margin + band, :],
        1.0,
        quot_real,
        quot_imag,
    )
    grad_scale = 2.0 * weights[kernel_index] * scale / total_kernels
    edge_cos = edge_pixels(col_cos, margin)
    edge_sin = edge_pixels(col_sin, margin)
    edges = grad_scale * (product(back_real, edge_cos) - product(back_imag, edge_sin))
    returned = padded(edges, (("tile", 1),), margin)
    centre_cos = col_cos[:, margin : margin + own_cols]
    centre_sin = col_sin[:, margin : margin + own_cols]
    centre = grad_scale * (product(back_real, centre_cos) - product(back_imag, centre_sin))
    own_grad = add_returned(centre, returned, margin)
    return exchange_sum(own_grad, "kern")


def solution(mesh):
    return jax.shard_map(
        body,
        mesh=mesh,
        in_specs=(
            P(None, "tile"),
            P("kern", None, None, None),
            P("kern"),
            P(None, "tile"),
            P(None, "tile"),
        ),
        out_specs=P(None, "tile"),
        check_vma=False,
    )
```

```python
import math

import jax
import jax.numpy as jnp
from jax import lax
from jax.sharding import PartitionSpec as P

BLK = 32


STEEPNESS = 6.0
THRESHOLD = 0.8


def padded(shard, sides, width):
    for axis, dim in sides:
        peers, length = (lax.axis_size(axis), shard.shape[dim])
        up = [(i, (i + 1) % peers) for i in range(peers - 1)]
        down = [(j, i) for i, j in up]
        last = lax.slice_in_dim(shard, length - width, length, axis=dim)
        initial = lax.slice_in_dim(shard, 0, width, axis=dim)
        before = lax.ppermute(last, axis, up)
        after = lax.ppermute(initial, axis, down)
        shard = jnp.concatenate([before, shard, after], axis=dim)
    return shard


def exchange_sum(value, axis):
    peers = lax.axis_size(axis)
    rows, cols = value.shape
    if (rows * cols) % peers:
        return lax.psum(value, axis)
    parts = value.reshape(peers, rows * cols // peers)
    parts = lax.all_to_all(parts, axis, 0, 0, tiled=True)
    total = jnp.sum(parts, axis=0, keepdims=True)
    gathered = lax.all_to_all(jnp.broadcast_to(total, parts.shape), axis, 0, 0, tiled=True)
    return gathered.reshape(rows, cols)


def product(left_mat, right_mat):
    return jnp.dot(
        left_mat, right_mat, precision=lax.Precision.HIGHEST, preferred_element_type=jnp.float32
    )


def twiddle(length):
    series = jnp.arange(length, dtype=jnp.int32)
    phase = series[:, None] * series[None, :] % length
    angle = phase.astype(jnp.float32) * (2.0 * math.pi / length)
    return (jnp.cos(angle), jnp.sin(angle))


def apply_left(cosine, sine, sign, real_part, imag_part):
    return (
        product(cosine, real_part) - sign * product(sine, imag_part),
        product(cosine, imag_part) + sign * product(sine, real_part),
    )


def apply_right(real_part, imag_part, cosine, sine, sign):
    return (
        product(real_part, cosine) - sign * product(imag_part, sine),
        product(imag_part, cosine) + sign * product(real_part, sine),
    )


def edge_pixels(frame, margin):
    return jnp.concatenate([frame[:, :margin], frame[:, frame.shape[1] - margin :]], axis=1)


def add_returned(own, returned, margin):
    from_left = returned[:, :margin]
    from_right = returned[:, returned.shape[1] - margin :]
    own = own.at[:, :margin].add(from_left)
    return own.at[:, own.shape[1] - margin :].add(from_right)


def resist_drive(intensity, target_rows, active_rows):
    resist = jax.nn.sigmoid(STEEPNESS * (intensity - THRESHOLD))
    return 2.0 * (resist - target_rows) * active_rows * STEEPNESS * resist * (1.0 - resist)


def body(mask, kernels, weights, target, active):
    band, own_cols = mask.shape
    width = kernels.shape[-1]
    margin = (width - 1) // 2
    frame_rows = band + 2 * margin
    frame_cols = own_cols + 2 * margin
    total_kernels = kernels.shape[0] * lax.axis_size("kern")
    scale = 1.0 / (frame_rows * frame_cols)
    row_cos, row_sin = twiddle(frame_rows)
    col_cos, col_sin = twiddle(frame_cols)
    extended = padded(mask, (("tile", 1),), margin)
    cols_real = product(extended, col_cos)
    cols_imag = -product(extended, col_sin)
    spec_real, spec_imag = apply_left(
        row_cos[:, margin : margin + band],
        row_sin[:, margin : margin + band],
        -1.0,
        cols_real,
        cols_imag,
    )
    kernel_index = 0
    kern_real, kern_imag = apply_left(
        row_cos[:, :width],
        row_sin[:, :width],
        1.0,
        kernels[kernel_index, 0],
        kernels[kernel_index, 1],
    )
    kern_real, kern_imag = apply_right(
        kern_real, kern_imag, col_cos[:width, :], col_sin[:width, :], 1.0
    )
    prod_real = spec_real * kern_real - spec_imag * kern_imag
    prod_imag = spec_real * kern_imag + spec_imag * kern_real
    field_real, field_imag = apply_left(
        row_cos[:band, :], row_sin[:band, :], 1.0, prod_real, prod_imag
    )
    field_real, field_imag = apply_right(
        field_real, field_imag, col_cos[:, :own_cols], col_sin[:, :own_cols], 1.0
    )
    field_real = field_real * scale
    field_imag = field_imag * scale
    responses = [(kern_real, kern_imag, field_real, field_imag)]
    share_sum = weights[kernel_index] * (field_real * field_real + field_imag * field_imag)
    share_sum = share_sum / total_kernels
    target_float = target.astype(jnp.float32)
    pixel_active = jnp.repeat(jnp.repeat(active, BLK, axis=0), BLK, axis=1).astype(jnp.float32)
    intensity = exchange_sum(share_sum, "kern")
    drive = resist_drive(intensity, target_float, pixel_active)
    kernel_index = 0
    kern_real, kern_imag, field_real, field_imag = responses[kernel_index]
    source_real, source_imag = apply_right(
        drive * field_real, drive * field_imag, col_cos[:own_cols, :], col_sin[:own_cols, :], -1.0
    )
    source_real, source_imag = apply_left(
        row_cos[:, :band], row_sin[:, :band], -1.0, source_real, source_imag
    )
    quot_real = source_real * kern_real + source_imag * kern_imag
    quot_imag = source_imag * kern_real - source_real * kern_imag
    back_real, back_imag = apply_left(
        row_cos[margin : margin + band, :],
        row_sin[margin : margin + band, :],
        1.0,
        quot_real,
        quot_imag,
    )
    grad_scale = 2.0 * weights[kernel_index] * scale / total_kernels
    edge_cos = edge_pixels(col_cos, margin)
    edge_sin = edge_pixels(col_sin, margin)
    edges = grad_scale * (product(back_real, edge_cos) - product(back_imag, edge_sin))
    returned = padded(edges, (("tile", 1),), margin)
    centre_cos = col_cos[:, margin : margin + own_cols]
    centre_sin = col_sin[:, margin : margin + own_cols]
    centre = grad_scale * (product(back_real, centre_cos) - product(back_imag, centre_sin))
    own_grad = add_returned(centre, returned, margin)
    return exchange_sum(own_grad, "kern")


def solution(mesh):
    return jax.shard_map(
        body,
        mesh=mesh,
        in_specs=(
            P(None, "tile"),
            P("kern", None, None, None),
            P("kern"),
            P(None, "tile"),
            P(None, "tile"),
        ),
        out_specs=P(None, "tile"),
        check_vma=False,
    )
```

```python
import math

import jax
import numpy as np
import jax.numpy as jnp
from jax import lax
from jax.sharding import PartitionSpec as P

BLK = 32


STEEPNESS = 6.0
THRESHOLD = 0.8


def padded(shard, sides, width):
    for axis, dim in sides:
        peers, length = (lax.axis_size(axis), shard.shape[dim])
        up = [(i, (i + 1) % peers) for i in range(peers - 1)]
        down = [(j, i) for i, j in up]
        last = lax.slice_in_dim(shard, length - width, length, axis=dim)
        initial = lax.slice_in_dim(shard, 0, width, axis=dim)
        before = lax.ppermute(last, axis, up)
        after = lax.ppermute(initial, axis, down)
        shard = jnp.concatenate([before, shard, after], axis=dim)
    return shard


def exchange_sum(value, axis):
    peers = lax.axis_size(axis)
    rows, cols = value.shape
    if (rows * cols) % peers:
        return lax.psum(value, axis)
    parts = value.reshape(peers, rows * cols // peers)
    parts = lax.all_to_all(parts, axis, 0, 0, tiled=True)
    total = jnp.sum(parts, axis=0, keepdims=True)
    gathered = lax.all_to_all(jnp.broadcast_to(total, parts.shape), axis, 0, 0, tiled=True)
    return gathered.reshape(rows, cols)


def product(left_mat, right_mat):
    return jnp.dot(
        left_mat, right_mat, precision=lax.Precision.HIGHEST, preferred_element_type=jnp.float32
    )


def twiddle(length):
    series = np.arange(length, dtype=np.int64)
    angle = (series[:, None] * series[None, :] % length) * (2.0 * math.pi / length)
    return (jnp.asarray(np.cos(angle), jnp.float32), jnp.asarray(np.sin(angle), jnp.float32))


def apply_left(cosine, sine, sign, real_part, imag_part):
    return (
        product(cosine, real_part) - sign * product(sine, imag_part),
        product(cosine, imag_part) + sign * product(sine, real_part),
    )


def apply_right(real_part, imag_part, cosine, sine, sign):
    return (
        product(real_part, cosine) - sign * product(imag_part, sine),
        product(imag_part, cosine) + sign * product(real_part, sine),
    )


def edge_pixels(frame, margin):
    return jnp.concatenate([frame[:, :margin], frame[:, frame.shape[1] - margin :]], axis=1)


def add_returned(own, returned, margin):
    from_left = returned[:, :margin]
    from_right = returned[:, returned.shape[1] - margin :]
    own = own.at[:, :margin].add(from_left)
    return own.at[:, own.shape[1] - margin :].add(from_right)


def resist_drive(intensity, target_rows, active_rows):
    resist = jax.nn.sigmoid(STEEPNESS * (intensity - THRESHOLD))
    return 2.0 * (resist - target_rows) * active_rows * STEEPNESS * resist * (1.0 - resist)


def body(mask, kernels, weights, target, active):
    band, own_cols = mask.shape
    width = kernels.shape[-1]
    margin = (width - 1) // 2
    frame_rows = band + 2 * margin
    frame_cols = own_cols + 2 * margin
    total_kernels = kernels.shape[0] * lax.axis_size("kern")
    scale = 1.0 / (frame_rows * frame_cols)
    row_cos, row_sin = twiddle(frame_rows)
    col_cos, col_sin = twiddle(frame_cols)
    row_cos, row_sin, col_cos, col_sin = lax.optimization_barrier((row_cos, row_sin, col_cos, col_sin))
    extended = padded(mask, (("tile", 1),), margin)
    cols_real = product(extended, col_cos)
    cols_imag = -product(extended, col_sin)
    spec_real, spec_imag = apply_left(
        row_cos[:, margin : margin + band],
        row_sin[:, margin : margin + band],
        -1.0,
        cols_real,
        cols_imag,
    )
    kernel_index = 0
    kern_real, kern_imag = apply_left(
        row_cos[:, :width],
        row_sin[:, :width],
        1.0,
        kernels[kernel_index, 0],
        kernels[kernel_index, 1],
    )
    kern_real, kern_imag = apply_right(
        kern_real, kern_imag, col_cos[:width, :], col_sin[:width, :], 1.0
    )
    prod_real = spec_real * kern_real - spec_imag * kern_imag
    prod_imag = spec_real * kern_imag + spec_imag * kern_real
    field_real, field_imag = apply_left(
        row_cos[:band, :], row_sin[:band, :], 1.0, prod_real, prod_imag
    )
    field_real, field_imag = apply_right(
        field_real, field_imag, col_cos[:, :own_cols], col_sin[:, :own_cols], 1.0
    )
    field_real = field_real * scale
    field_imag = field_imag * scale
    responses = [(kern_real, kern_imag, field_real, field_imag)]
    share_sum = weights[kernel_index] * (field_real * field_real + field_imag * field_imag)
    share_sum = share_sum / total_kernels
    target_float = target.astype(jnp.float32)
    pixel_active = jnp.repeat(jnp.repeat(active, BLK, axis=0), BLK, axis=1).astype(jnp.float32)
    intensity = exchange_sum(share_sum, "kern")
    drive = resist_drive(intensity, target_float, pixel_active)
    kernel_index = 0
    kern_real, kern_imag, field_real, field_imag = responses[kernel_index]
    source_real, source_imag = apply_right(
        drive * field_real, drive * field_imag, col_cos[:own_cols, :], col_sin[:own_cols, :], -1.0
    )
    source_real, source_imag = apply_left(
        row_cos[:, :band], row_sin[:, :band], -1.0, source_real, source_imag
    )
    quot_real = source_real * kern_real + source_imag * kern_imag
    quot_imag = source_imag * kern_real - source_real * kern_imag
    back_real, back_imag = apply_left(
        row_cos[margin : margin + band, :],
        row_sin[margin : margin + band, :],
        1.0,
        quot_real,
        quot_imag,
    )
    grad_scale = 2.0 * weights[kernel_index] * scale / total_kernels
    edge_cos = edge_pixels(col_cos, margin)
    edge_sin = edge_pixels(col_sin, margin)
    edges = grad_scale * (product(back_real, edge_cos) - product(back_imag, edge_sin))
    returned = padded(edges, (("tile", 1),), margin)
    centre_cos = col_cos[:, margin : margin + own_cols]
    centre_sin = col_sin[:, margin : margin + own_cols]
    centre = grad_scale * (product(back_real, centre_cos) - product(back_imag, centre_sin))
    own_grad = add_returned(centre, returned, margin)
    return exchange_sum(own_grad, "kern")


def solution(mesh):
    return jax.shard_map(
        body,
        mesh=mesh,
        in_specs=(
            P(None, "tile"),
            P("kern", None, None, None),
            P("kern"),
            P(None, "tile"),
            P(None, "tile"),
        ),
        out_specs=P(None, "tile"),
        check_vma=False,
    )
```

```python
import math

import jax
import numpy as np
import jax.numpy as jnp
from jax import lax
from jax.sharding import PartitionSpec as P

BLK = 32


STEEPNESS = 6.0
THRESHOLD = 0.8


def padded(shard, sides, width):
    for axis, dim in sides:
        peers, length = (lax.axis_size(axis), shard.shape[dim])
        up = [(i, (i + 1) % peers) for i in range(peers - 1)]
        down = [(j, i) for i, j in up]
        last = lax.slice_in_dim(shard, length - width, length, axis=dim)
        initial = lax.slice_in_dim(shard, 0, width, axis=dim)
        before = lax.ppermute(last, axis, up)
        after = lax.ppermute(initial, axis, down)
        shard = jnp.concatenate([before, shard, after], axis=dim)
    return shard


def exchange_sum(value, axis):
    peers = lax.axis_size(axis)
    rows, cols = value.shape
    if (rows * cols) % peers:
        return lax.psum(value, axis)
    parts = value.reshape(peers, rows * cols // peers)
    parts = lax.all_to_all(parts, axis, 0, 0, tiled=True)
    total = jnp.sum(parts, axis=0, keepdims=True)
    gathered = lax.all_to_all(jnp.broadcast_to(total, parts.shape), axis, 0, 0, tiled=True)
    return gathered.reshape(rows, cols)


def product(left_mat, right_mat):
    return jnp.dot(
        left_mat, right_mat, precision=lax.Precision.HIGHEST, preferred_element_type=jnp.float32
    )


def twiddle(length):
    series = np.arange(length, dtype=np.int64)
    angle = (series[:, None] * series[None, :] % length) * (2.0 * math.pi / length)
    return (jnp.asarray(np.cos(angle), jnp.float32), jnp.asarray(np.sin(angle), jnp.float32))


def apply_left(cosine, sine, sign, real_part, imag_part):
    return (
        product(cosine, real_part) - sign * product(sine, imag_part),
        product(cosine, imag_part) + sign * product(sine, real_part),
    )


def apply_right(real_part, imag_part, cosine, sine, sign):
    return (
        product(real_part, cosine) - sign * product(imag_part, sine),
        product(imag_part, cosine) + sign * product(real_part, sine),
    )


def edge_pixels(frame, margin):
    return jnp.concatenate([frame[:, :margin], frame[:, frame.shape[1] - margin :]], axis=1)


def add_returned(own, returned, margin):
    from_left = returned[:, :margin]
    from_right = returned[:, returned.shape[1] - margin :]
    own = own.at[:, :margin].add(from_left)
    return own.at[:, own.shape[1] - margin :].add(from_right)


def resist_drive(intensity, target_rows, active_rows):
    resist = jax.nn.sigmoid(STEEPNESS * (intensity - THRESHOLD))
    return 2.0 * (resist - target_rows) * active_rows * STEEPNESS * resist * (1.0 - resist)


def body(mask, kernels, weights, target, active):
    band, own_cols = mask.shape
    width = kernels.shape[-1]
    margin = (width - 1) // 2
    reach = 2 * margin
    field_cols = own_cols + reach
    frame_rows = band + 2 * margin
    frame_cols = own_cols + 2 * reach
    total_kernels = kernels.shape[0] * lax.axis_size("kern")
    scale = 1.0 / (frame_rows * frame_cols)
    row_cos, row_sin = twiddle(frame_rows)
    col_cos, col_sin = twiddle(frame_cols)
    row_cos, row_sin, col_cos, col_sin = lax.optimization_barrier((row_cos, row_sin, col_cos, col_sin))
    extended = padded(mask, (("tile", 1),), reach)
    block_cols = own_cols // active.shape[1]
    target_ext = padded(target.astype(jnp.float32), (("tile", 1),), margin)
    active_ext = padded(active.astype(jnp.float32), (("tile", 1),), margin // block_cols)
    cols_real = product(extended, col_cos)
    cols_imag = -product(extended, col_sin)
    spec_real, spec_imag = apply_left(
        row_cos[:, margin : margin + band],
        row_sin[:, margin : margin + band],
        -1.0,
        cols_real,
        cols_imag,
    )
    kernel_index = 0
    kern_real, kern_imag = apply_left(
        row_cos[:, :width],
        row_sin[:, :width],
        1.0,
        kernels[kernel_index, 0],
        kernels[kernel_index, 1],
    )
    kern_real, kern_imag = apply_right(
        kern_real, kern_imag, col_cos[:width, :], col_sin[:width, :], 1.0
    )
    prod_real = spec_real * kern_real - spec_imag * kern_imag
    prod_imag = spec_real * kern_imag + spec_imag * kern_real
    field_real, field_imag = apply_left(
        row_cos[:band, :], row_sin[:band, :], 1.0, prod_real, prod_imag
    )
    field_real, field_imag = apply_right(
        field_real, field_imag, col_cos[:, :field_cols], col_sin[:, :field_cols], 1.0
    )
    field_real = field_real * scale
    field_imag = field_imag * scale
    share_sum = weights[kernel_index] * (field_real * field_real + field_imag * field_imag)
    share_sum = share_sum / total_kernels
    pixel_active = jnp.repeat(jnp.repeat(active_ext, BLK, axis=0), block_cols, axis=1)
    intensity = exchange_sum(share_sum, "kern")
    drive = resist_drive(intensity, target_ext, pixel_active)
    source_real, source_imag = apply_right(
        drive * field_real,
        drive * field_imag,
        col_cos[:field_cols, :],
        col_sin[:field_cols, :],
        -1.0,
    )
    source_real, source_imag = apply_left(
        row_cos[:, :band], row_sin[:, :band], -1.0, source_real, source_imag
    )
    quot_real = source_real * kern_real + source_imag * kern_imag
    quot_imag = source_imag * kern_real - source_real * kern_imag
    back_real, back_imag = apply_left(
        row_cos[margin : margin + band, :],
        row_sin[margin : margin + band, :],
        1.0,
        quot_real,
        quot_imag,
    )
    grad_scale = 2.0 * weights[kernel_index] * scale / total_kernels
    own_cos = col_cos[:, reach : reach + own_cols]
    own_sin = col_sin[:, reach : reach + own_cols]
    own_grad = grad_scale * (product(back_real, own_cos) - product(back_imag, own_sin))
    return exchange_sum(own_grad, "kern")


def solution(mesh):
    return jax.shard_map(
        body,
        mesh=mesh,
        in_specs=(
            P(None, "tile"),
            P("kern", None, None, None),
            P("kern"),
            P(None, "tile"),
            P(None, "tile"),
        ),
        out_specs=P(None, "tile"),
        check_vma=False,
    )
```

```python
import math

import jax
import numpy as np
import jax.numpy as jnp
from jax import lax
from jax.sharding import PartitionSpec as P

BLK = 32


STEEPNESS = 6.0
THRESHOLD = 0.8


def padded(shard, sides, width):
    for axis, dim in sides:
        peers, length = (lax.axis_size(axis), shard.shape[dim])
        up = [(i, (i + 1) % peers) for i in range(peers - 1)]
        down = [(j, i) for i, j in up]
        last = lax.slice_in_dim(shard, length - width, length, axis=dim)
        initial = lax.slice_in_dim(shard, 0, width, axis=dim)
        before = lax.ppermute(last, axis, up)
        after = lax.ppermute(initial, axis, down)
        shard = jnp.concatenate([before, shard, after], axis=dim)
    return shard


def exchange_sum(value, axis):
    peers = lax.axis_size(axis)
    rows, cols = value.shape
    if (rows * cols) % peers:
        return lax.psum(value, axis)
    parts = value.reshape(peers, rows * cols // peers)
    parts = lax.all_to_all(parts, axis, 0, 0, tiled=True)
    total = jnp.sum(parts, axis=0, keepdims=True)
    gathered = lax.all_to_all(jnp.broadcast_to(total, parts.shape), axis, 0, 0, tiled=True)
    return gathered.reshape(rows, cols)


def product(left_mat, right_mat):
    return jnp.dot(
        left_mat, right_mat, precision=lax.Precision.HIGHEST, preferred_element_type=jnp.float32
    )


def twiddle(length):
    series = np.arange(length, dtype=np.int64)
    angle = (series[:, None] * series[None, :] % length) * (2.0 * math.pi / length)
    return (jnp.asarray(np.cos(angle), jnp.float32), jnp.asarray(np.sin(angle), jnp.float32))


def apply_left(cosine, sine, sign, real_part, imag_part):
    return (
        product(cosine, real_part) - sign * product(sine, imag_part),
        product(cosine, imag_part) + sign * product(sine, real_part),
    )


def apply_right(real_part, imag_part, cosine, sine, sign):
    return (
        product(real_part, cosine) - sign * product(imag_part, sine),
        product(imag_part, cosine) + sign * product(real_part, sine),
    )


def edge_pixels(frame, margin):
    return jnp.concatenate([frame[:, :margin], frame[:, frame.shape[1] - margin :]], axis=1)


def add_returned(own, returned, margin):
    from_left = returned[:, :margin]
    from_right = returned[:, returned.shape[1] - margin :]
    own = own.at[:, :margin].add(from_left)
    return own.at[:, own.shape[1] - margin :].add(from_right)


def resist_drive(intensity, target_rows, active_rows):
    resist = jax.nn.sigmoid(STEEPNESS * (intensity - THRESHOLD))
    return 2.0 * (resist - target_rows) * active_rows * STEEPNESS * resist * (1.0 - resist)


def body(mask, kernels, weights, target, active):
    band, own_cols = mask.shape
    width = kernels.shape[-1]
    margin = (width - 1) // 2
    reach = 2 * margin
    field_cols = own_cols + reach
    frame_rows = band + 2 * margin
    frame_cols = own_cols + 2 * reach
    total_kernels = kernels.shape[0] * lax.axis_size("kern")
    scale = 1.0 / (frame_rows * frame_cols)
    row_cos, row_sin = twiddle(frame_rows)
    col_cos, col_sin = twiddle(frame_cols)
    row_cos, row_sin, col_cos, col_sin = lax.optimization_barrier((row_cos, row_sin, col_cos, col_sin))
    block_rows = band // active.shape[0]
    block_cols = own_cols // active.shape[1]
    own_active = jnp.repeat(jnp.repeat(active, block_rows, axis=0), block_cols, axis=1)
    stacked = jnp.concatenate(
        [mask, target.astype(jnp.float32), own_active.astype(jnp.float32)], axis=0
    )
    stacked = padded(stacked, (("tile", 1),), reach)
    extended = stacked[:band]
    target_ext = stacked[band : 2 * band, margin : margin + field_cols]
    pixel_active = stacked[2 * band :, margin : margin + field_cols]
    cols_real = product(extended, col_cos)
    cols_imag = -product(extended, col_sin)
    spec_real, spec_imag = apply_left(
        row_cos[:, margin : margin + band],
        row_sin[:, margin : margin + band],
        -1.0,
        cols_real,
        cols_imag,
    )
    kernel_index = 0
    kern_real, kern_imag = apply_left(
        row_cos[:, :width],
        row_sin[:, :width],
        1.0,
        kernels[kernel_index, 0],
        kernels[kernel_index, 1],
    )
    kern_real, kern_imag = apply_right(
        kern_real, kern_imag, col_cos[:width, :], col_sin[:width, :], 1.0
    )
    prod_real = spec_real * kern_real - spec_imag * kern_imag
    prod_imag = spec_real * kern_imag + spec_imag * kern_real
    field_real, field_imag = apply_left(
        row_cos[:band, :], row_sin[:band, :], 1.0, prod_real, prod_imag
    )
    field_real, field_imag = apply_right(
        field_real, field_imag, col_cos[:, :field_cols], col_sin[:, :field_cols], 1.0
    )
    field_real = field_real * scale
    field_imag = field_imag * scale
    share_sum = weights[kernel_index] * (field_real * field_real + field_imag * field_imag)
    share_sum = share_sum / total_kernels
    intensity = exchange_sum(share_sum, "kern")
    drive = resist_drive(intensity, target_ext, pixel_active)
    source_real, source_imag = apply_right(
        drive * field_real,
        drive * field_imag,
        col_cos[:field_cols, :],
        col_sin[:field_cols, :],
        -1.0,
    )
    source_real, source_imag = apply_left(
        row_cos[:, :band], row_sin[:, :band], -1.0, source_real, source_imag
    )
    quot_real = source_real * kern_real + source_imag * kern_imag
    quot_imag = source_imag * kern_real - source_real * kern_imag
    back_real, back_imag = apply_left(
        row_cos[margin : margin + band, :],
        row_sin[margin : margin + band, :],
        1.0,
        quot_real,
        quot_imag,
    )
    grad_scale = 2.0 * weights[kernel_index] * scale / total_kernels
    own_cos = col_cos[:, reach : reach + own_cols]
    own_sin = col_sin[:, reach : reach + own_cols]
    own_grad = grad_scale * (product(back_real, own_cos) - product(back_imag, own_sin))
    return exchange_sum(own_grad, "kern")


def solution(mesh):
    return jax.shard_map(
        body,
        mesh=mesh,
        in_specs=(
            P(None, "tile"),
            P("kern", None, None, None),
            P("kern"),
            P(None, "tile"),
            P(None, "tile"),
        ),
        out_specs=P(None, "tile"),
        check_vma=False,
    )
```

```python
import math

import jax
import numpy as np
import jax.numpy as jnp
from jax import lax
from jax.sharding import PartitionSpec as P

BLK = 32


STEEPNESS = 6.0
THRESHOLD = 0.8


def padded(shard, sides, width):
    for axis, dim in sides:
        peers, length = (lax.axis_size(axis), shard.shape[dim])
        up = [(i, (i + 1) % peers) for i in range(peers - 1)]
        down = [(j, i) for i, j in up]
        last = lax.slice_in_dim(shard, length - width, length, axis=dim)
        initial = lax.slice_in_dim(shard, 0, width, axis=dim)
        before = lax.ppermute(last, axis, up)
        after = lax.ppermute(initial, axis, down)
        shard = jnp.concatenate([before, shard, after], axis=dim)
    return shard


def exchange_sum(value, axis):
    peers = lax.axis_size(axis)
    rows, cols = value.shape
    if (rows * cols) % peers:
        return lax.psum(value, axis)
    parts = value.reshape(peers, rows * cols // peers)
    parts = lax.all_to_all(parts, axis, 0, 0, tiled=True)
    total = jnp.sum(parts, axis=0, keepdims=True)
    gathered = lax.all_to_all(jnp.broadcast_to(total, parts.shape), axis, 0, 0, tiled=True)
    return gathered.reshape(rows, cols)


def product(left_mat, right_mat):
    return jnp.dot(
        left_mat, right_mat, precision=lax.Precision.HIGHEST, preferred_element_type=jnp.float32
    )


def twiddle(length):
    series = np.arange(length, dtype=np.int64)
    angle = (series[:, None] * series[None, :] % length) * (2.0 * math.pi / length)
    return (jnp.asarray(np.cos(angle), jnp.float32), jnp.asarray(np.sin(angle), jnp.float32))


def apply_left(cosine, sine, sign, real_part, imag_part):
    width = real_part.shape[1]
    both = jnp.concatenate([real_part, imag_part], axis=1)
    by_cos = product(cosine, both)
    by_sin = product(sine, both)
    return (
        by_cos[:, :width] - sign * by_sin[:, width:],
        by_cos[:, width:] + sign * by_sin[:, :width],
    )


def apply_right(real_part, imag_part, cosine, sine, sign):
    height = real_part.shape[0]
    both = jnp.concatenate([real_part, imag_part], axis=0)
    by_cos = product(both, cosine)
    by_sin = product(both, sine)
    return (
        by_cos[:height] - sign * by_sin[height:],
        by_cos[height:] + sign * by_sin[:height],
    )


def edge_pixels(frame, margin):
    return jnp.concatenate([frame[:, :margin], frame[:, frame.shape[1] - margin :]], axis=1)


def add_returned(own, returned, margin):
    from_left = returned[:, :margin]
    from_right = returned[:, returned.shape[1] - margin :]
    own = own.at[:, :margin].add(from_left)
    return own.at[:, own.shape[1] - margin :].add(from_right)


def resist_drive(intensity, target_rows, active_rows):
    resist = jax.nn.sigmoid(STEEPNESS * (intensity - THRESHOLD))
    return 2.0 * (resist - target_rows) * active_rows * STEEPNESS * resist * (1.0 - resist)


def body(mask, kernels, weights, target, active):
    band, own_cols = mask.shape
    width = kernels.shape[-1]
    margin = (width - 1) // 2
    reach = 2 * margin
    field_cols = own_cols + reach
    frame_rows = band + 2 * margin
    frame_cols = own_cols + 2 * reach
    total_kernels = kernels.shape[0] * lax.axis_size("kern")
    scale = 1.0 / (frame_rows * frame_cols)
    row_cos, row_sin = twiddle(frame_rows)
    col_cos, col_sin = twiddle(frame_cols)
    row_cos, row_sin, col_cos, col_sin = lax.optimization_barrier((row_cos, row_sin, col_cos, col_sin))
    block_rows = band // active.shape[0]
    block_cols = own_cols // active.shape[1]
    own_active = jnp.repeat(jnp.repeat(active, block_rows, axis=0), block_cols, axis=1)
    stacked = jnp.concatenate(
        [mask, target.astype(jnp.float32), own_active.astype(jnp.float32)], axis=0
    )
    stacked = padded(stacked, (("tile", 1),), reach)
    extended = stacked[:band]
    target_ext = stacked[band : 2 * band, margin : margin + field_cols]
    pixel_active = stacked[2 * band :, margin : margin + field_cols]
    cols_real = product(extended, col_cos)
    cols_imag = -product(extended, col_sin)
    spec_real, spec_imag = apply_left(
        row_cos[:, margin : margin + band],
        row_sin[:, margin : margin + band],
        -1.0,
        cols_real,
        cols_imag,
    )
    kernel_index = 0
    kern_real, kern_imag = apply_left(
        row_cos[:, :width],
        row_sin[:, :width],
        1.0,
        kernels[kernel_index, 0],
        kernels[kernel_index, 1],
    )
    kern_real, kern_imag = apply_right(
        kern_real, kern_imag, col_cos[:width, :], col_sin[:width, :], 1.0
    )
    prod_real = spec_real * kern_real - spec_imag * kern_imag
    prod_imag = spec_real * kern_imag + spec_imag * kern_real
    field_real, field_imag = apply_left(
        row_cos[:band, :], row_sin[:band, :], 1.0, prod_real, prod_imag
    )
    field_real, field_imag = apply_right(
        field_real, field_imag, col_cos[:, :field_cols], col_sin[:, :field_cols], 1.0
    )
    field_real = field_real * scale
    field_imag = field_imag * scale
    share_sum = weights[kernel_index] * (field_real * field_real + field_imag * field_imag)
    share_sum = share_sum / total_kernels
    intensity = exchange_sum(share_sum, "kern")
    drive = resist_drive(intensity, target_ext, pixel_active)
    source_real, source_imag = apply_right(
        drive * field_real,
        drive * field_imag,
        col_cos[:field_cols, :],
        col_sin[:field_cols, :],
        -1.0,
    )
    source_real, source_imag = apply_left(
        row_cos[:, :band], row_sin[:, :band], -1.0, source_real, source_imag
    )
    quot_real = source_real * kern_real + source_imag * kern_imag
    quot_imag = source_imag * kern_real - source_real * kern_imag
    back_real, back_imag = apply_left(
        row_cos[margin : margin + band, :],
        row_sin[margin : margin + band, :],
        1.0,
        quot_real,
        quot_imag,
    )
    grad_scale = 2.0 * weights[kernel_index] * scale / total_kernels
    own_cos = col_cos[:, reach : reach + own_cols]
    own_sin = col_sin[:, reach : reach + own_cols]
    own_grad = grad_scale * (product(back_real, own_cos) - product(back_imag, own_sin))
    return exchange_sum(own_grad, "kern")


def solution(mesh):
    return jax.shard_map(
        body,
        mesh=mesh,
        in_specs=(
            P(None, "tile"),
            P("kern", None, None, None),
            P("kern"),
            P(None, "tile"),
            P(None, "tile"),
        ),
        out_specs=P(None, "tile"),
        check_vma=False,
    )
```

```python
import math

import jax
import numpy as np
import jax.numpy as jnp
from jax import lax
from jax.sharding import PartitionSpec as P

BLK = 32


STEEPNESS = 6.0
THRESHOLD = 0.8


def padded(shard, sides, width):
    for axis, dim in sides:
        peers, length = (lax.axis_size(axis), shard.shape[dim])
        up = [(i, (i + 1) % peers) for i in range(peers - 1)]
        down = [(j, i) for i, j in up]
        last = lax.slice_in_dim(shard, length - width, length, axis=dim)
        initial = lax.slice_in_dim(shard, 0, width, axis=dim)
        before = lax.ppermute(last, axis, up)
        after = lax.ppermute(initial, axis, down)
        shard = jnp.concatenate([before, shard, after], axis=dim)
    return shard


def exchange_sum(value, axis):
    peers = lax.axis_size(axis)
    rows, cols = value.shape
    if (rows * cols) % peers:
        return lax.psum(value, axis)
    parts = value.reshape(peers, rows * cols // peers)
    parts = lax.all_to_all(parts, axis, 0, 0, tiled=True)
    total = jnp.sum(parts, axis=0, keepdims=True)
    gathered = lax.all_to_all(jnp.broadcast_to(total, parts.shape), axis, 0, 0, tiled=True)
    return gathered.reshape(rows, cols)


def product(left_mat, right_mat):
    return jnp.dot(
        left_mat, right_mat, precision=lax.Precision.HIGHEST, preferred_element_type=jnp.float32
    )


def twiddle(length):
    series = np.arange(length, dtype=np.int64)
    angle = (series[:, None] * series[None, :] % length) * (2.0 * math.pi / length)
    return (jnp.asarray(np.cos(angle), jnp.float32), jnp.asarray(np.sin(angle), jnp.float32))


def apply_left(cosine, sine, sign, real_part, imag_part):
    width = real_part.shape[1]
    both = jnp.concatenate([real_part, imag_part], axis=1)
    by_cos = product(cosine, both)
    by_sin = product(sine, both)
    return (
        by_cos[:, :width] - sign * by_sin[:, width:],
        by_cos[:, width:] + sign * by_sin[:, :width],
    )


def apply_right(real_part, imag_part, cosine, sine, sign):
    height = real_part.shape[0]
    both = jnp.concatenate([real_part, imag_part], axis=0)
    by_cos = product(both, cosine)
    by_sin = product(both, sine)
    return (
        by_cos[:height] - sign * by_sin[height:],
        by_cos[height:] + sign * by_sin[:height],
    )


def left_stacked(stack, sign, real_part, imag_part):
    height = stack.shape[0] // 2
    width = real_part.shape[1]
    full = product(stack, jnp.concatenate([real_part, imag_part], axis=1))
    return (
        full[:height, :width] - sign * full[height:, width:],
        full[:height, width:] + sign * full[height:, :width],
    )


def right_stacked(real_part, imag_part, stack, sign):
    height = real_part.shape[0]
    width = stack.shape[1] // 2
    full = product(jnp.concatenate([real_part, imag_part], axis=0), stack)
    return (
        full[:height, :width] - sign * full[height:, width:],
        full[height:, :width] + sign * full[:height, width:],
    )


def edge_pixels(frame, margin):
    return jnp.concatenate([frame[:, :margin], frame[:, frame.shape[1] - margin :]], axis=1)


def add_returned(own, returned, margin):
    from_left = returned[:, :margin]
    from_right = returned[:, returned.shape[1] - margin :]
    own = own.at[:, :margin].add(from_left)
    return own.at[:, own.shape[1] - margin :].add(from_right)


def resist_drive(intensity, target_rows, active_rows):
    resist = jax.nn.sigmoid(STEEPNESS * (intensity - THRESHOLD))
    return 2.0 * (resist - target_rows) * active_rows * STEEPNESS * resist * (1.0 - resist)


def body(mask, kernels, weights, target, active):
    band, own_cols = mask.shape
    width = kernels.shape[-1]
    margin = (width - 1) // 2
    reach = 2 * margin
    field_cols = own_cols + reach
    frame_rows = band + 2 * margin
    frame_cols = own_cols + 2 * reach
    total_kernels = kernels.shape[0] * lax.axis_size("kern")
    scale = 1.0 / (frame_rows * frame_cols)
    row_cos, row_sin = twiddle(frame_rows)
    col_cos, col_sin = twiddle(frame_cols)
    row_stack = jnp.concatenate([row_cos, row_sin], axis=0)
    col_stack = jnp.concatenate([col_cos, col_sin], axis=1)
    row_stack, col_stack = lax.optimization_barrier((row_stack, col_stack))
    row_cos, row_sin = row_stack[:frame_rows], row_stack[frame_rows:]
    col_cos, col_sin = col_stack[:, :frame_cols], col_stack[:, frame_cols:]
    block_rows = band // active.shape[0]
    block_cols = own_cols // active.shape[1]
    own_active = jnp.repeat(jnp.repeat(active, block_rows, axis=0), block_cols, axis=1)
    stacked = jnp.concatenate(
        [mask, target.astype(jnp.float32), own_active.astype(jnp.float32)], axis=0
    )
    stacked = padded(stacked, (("tile", 1),), reach)
    extended = stacked[:band]
    target_ext = stacked[band : 2 * band, margin : margin + field_cols]
    pixel_active = stacked[2 * band :, margin : margin + field_cols]
    by_cols = product(extended, col_stack)
    cols_real = by_cols[:, :frame_cols]
    cols_imag = -by_cols[:, frame_cols:]
    spec_real, spec_imag = left_stacked(
        row_stack[:, margin : margin + band], -1.0, cols_real, cols_imag
    )
    kernel_index = 0
    kern_real, kern_imag = left_stacked(
        row_stack[:, :width], 1.0, kernels[kernel_index, 0], kernels[kernel_index, 1]
    )
    kern_real, kern_imag = right_stacked(kern_real, kern_imag, col_stack[:width, :], 1.0)
    prod_real = spec_real * kern_real - spec_imag * kern_imag
    prod_imag = spec_real * kern_imag + spec_imag * kern_real
    field_real, field_imag = apply_left(
        row_cos[:band, :], row_sin[:band, :], 1.0, prod_real, prod_imag
    )
    field_real, field_imag = apply_right(
        field_real, field_imag, col_cos[:, :field_cols], col_sin[:, :field_cols], 1.0
    )
    field_real = field_real * scale
    field_imag = field_imag * scale
    share_sum = weights[kernel_index] * (field_real * field_real + field_imag * field_imag)
    share_sum = share_sum / total_kernels
    intensity = exchange_sum(share_sum, "kern")
    drive = resist_drive(intensity, target_ext, pixel_active)
    source_real, source_imag = right_stacked(
        drive * field_real, drive * field_imag, col_stack[:field_cols, :], -1.0
    )
    source_real, source_imag = left_stacked(
        row_stack[:, :band], -1.0, source_real, source_imag
    )
    quot_real = source_real * kern_real + source_imag * kern_imag
    quot_imag = source_imag * kern_real - source_real * kern_imag
    back_real, back_imag = apply_left(
        row_cos[margin : margin + band, :],
        row_sin[margin : margin + band, :],
        1.0,
        quot_real,
        quot_imag,
    )
    grad_scale = 2.0 * weights[kernel_index] * scale / total_kernels
    own_cos = col_cos[:, reach : reach + own_cols]
    own_sin = col_sin[:, reach : reach + own_cols]
    own_grad = grad_scale * (product(back_real, own_cos) - product(back_imag, own_sin))
    return exchange_sum(own_grad, "kern")


def solution(mesh):
    return jax.shard_map(
        body,
        mesh=mesh,
        in_specs=(
            P(None, "tile"),
            P("kern", None, None, None),
            P("kern"),
            P(None, "tile"),
            P(None, "tile"),
        ),
        out_specs=P(None, "tile"),
        check_vma=False,
    )
```

```python
import math

import jax
import numpy as np
import jax.numpy as jnp
from jax import lax
from jax.sharding import PartitionSpec as P

BLK = 32


STEEPNESS = 6.0
THRESHOLD = 0.8


def padded(shard, sides, width):
    for axis, dim in sides:
        peers, length = (lax.axis_size(axis), shard.shape[dim])
        up = [(i, (i + 1) % peers) for i in range(peers - 1)]
        down = [(j, i) for i, j in up]
        last = lax.slice_in_dim(shard, length - width, length, axis=dim)
        initial = lax.slice_in_dim(shard, 0, width, axis=dim)
        before = lax.ppermute(last, axis, up)
        after = lax.ppermute(initial, axis, down)
        shard = jnp.concatenate([before, shard, after], axis=dim)
    return shard


def exchange_sum(value, axis):
    peers = lax.axis_size(axis)
    rows, cols = value.shape
    if (rows * cols) % peers:
        return lax.psum(value, axis)
    parts = value.reshape(peers, rows * cols // peers)
    parts = lax.all_to_all(parts, axis, 0, 0, tiled=True)
    total = jnp.sum(parts, axis=0, keepdims=True)
    gathered = lax.all_to_all(jnp.broadcast_to(total, parts.shape), axis, 0, 0, tiled=True)
    return gathered.reshape(rows, cols)


def product(left_mat, right_mat):
    return jnp.dot(
        left_mat, right_mat, precision=lax.Precision.HIGHEST, preferred_element_type=jnp.float32
    )


def twiddle(length):
    series = np.arange(length, dtype=np.int64)
    angle = (series[:, None] * series[None, :] % length) * (2.0 * math.pi / length)
    return (jnp.asarray(np.cos(angle), jnp.float32), jnp.asarray(np.sin(angle), jnp.float32))


def apply_left(cosine, sine, sign, real_part, imag_part):
    width = real_part.shape[1]
    both = jnp.concatenate([real_part, imag_part], axis=1)
    by_cos = product(cosine, both)
    by_sin = product(sine, both)
    return (
        by_cos[:, :width] - sign * by_sin[:, width:],
        by_cos[:, width:] + sign * by_sin[:, :width],
    )


def apply_right(real_part, imag_part, cosine, sine, sign):
    height = real_part.shape[0]
    both = jnp.concatenate([real_part, imag_part], axis=0)
    by_cos = product(both, cosine)
    by_sin = product(both, sine)
    return (
        by_cos[:height] - sign * by_sin[height:],
        by_cos[height:] + sign * by_sin[:height],
    )


def left_stacked(stack, sign, real_part, imag_part):
    height = stack.shape[0] // 2
    width = real_part.shape[1]
    full = product(stack, jnp.concatenate([real_part, imag_part], axis=1))
    return (
        full[:height, :width] - sign * full[height:, width:],
        full[:height, width:] + sign * full[height:, :width],
    )


def right_stacked(real_part, imag_part, stack, sign):
    height = real_part.shape[0]
    width = stack.shape[1] // 2
    full = product(jnp.concatenate([real_part, imag_part], axis=0), stack)
    return (
        full[:height, :width] - sign * full[height:, width:],
        full[height:, :width] + sign * full[:height, width:],
    )


def edge_pixels(frame, margin):
    return jnp.concatenate([frame[:, :margin], frame[:, frame.shape[1] - margin :]], axis=1)


def add_returned(own, returned, margin):
    from_left = returned[:, :margin]
    from_right = returned[:, returned.shape[1] - margin :]
    own = own.at[:, :margin].add(from_left)
    return own.at[:, own.shape[1] - margin :].add(from_right)


def resist_drive(intensity, target_rows, active_rows):
    resist = jax.nn.sigmoid(STEEPNESS * (intensity - THRESHOLD))
    return 2.0 * (resist - target_rows) * active_rows * STEEPNESS * resist * (1.0 - resist)


def body(mask, kernels, weights, target, active):
    band, own_cols = mask.shape
    width = kernels.shape[-1]
    margin = (width - 1) // 2
    reach = 2 * margin
    field_cols = own_cols + reach
    frame_rows = band + 2 * margin
    frame_cols = own_cols + 2 * reach
    total_kernels = kernels.shape[0] * lax.axis_size("kern")
    scale = 1.0 / (frame_rows * frame_cols)
    row_cos, row_sin = twiddle(frame_rows)
    col_cos, col_sin = twiddle(frame_cols)
    row_stack = jnp.concatenate([row_cos, row_sin], axis=0)
    col_stack = jnp.concatenate([col_cos, col_sin], axis=1)
    row_stack, col_stack = lax.optimization_barrier((row_stack, col_stack))
    row_cos, row_sin = row_stack[:frame_rows], row_stack[frame_rows:]
    col_cos, col_sin = col_stack[:, :frame_cols], col_stack[:, frame_cols:]
    block_grid, blocks = active.shape
    block_rows = band // block_grid
    block_cols = own_cols // blocks
    reach_blocks = margin // block_cols
    active_rows = jnp.pad(active.astype(jnp.float32), ((0, 0), (0, own_cols - blocks)))
    stacked = jnp.concatenate([mask, target.astype(jnp.float32), active_rows], axis=0)
    stacked = padded(stacked, (("tile", 1),), reach)
    extended = stacked[:band]
    target_ext = stacked[band : 2 * band, margin : margin + field_cols]
    active_row = stacked[2 * band :]
    active_ext = jnp.concatenate(
        [
            active_row[:, blocks - reach_blocks : blocks],
            active_row[:, own_cols : own_cols + blocks],
            active_row[:, 2 * own_cols : 2 * own_cols + reach_blocks],
        ],
        axis=1,
    )
    pixel_active = jnp.repeat(jnp.repeat(active_ext, block_rows, axis=0), block_cols, axis=1)
    by_cols = product(extended, col_stack)
    cols_real = by_cols[:, :frame_cols]
    cols_imag = -by_cols[:, frame_cols:]
    spec_real, spec_imag = left_stacked(
        row_stack[:, margin : margin + band], -1.0, cols_real, cols_imag
    )
    kernel_index = 0
    kern_real, kern_imag = left_stacked(
        row_stack[:, :width], 1.0, kernels[kernel_index, 0], kernels[kernel_index, 1]
    )
    kern_real, kern_imag = right_stacked(kern_real, kern_imag, col_stack[:width, :], 1.0)
    prod_real = spec_real * kern_real - spec_imag * kern_imag
    prod_imag = spec_real * kern_imag + spec_imag * kern_real
    field_real, field_imag = apply_left(
        row_cos[:band, :], row_sin[:band, :], 1.0, prod_real, prod_imag
    )
    field_real, field_imag = apply_right(
        field_real, field_imag, col_cos[:, :field_cols], col_sin[:, :field_cols], 1.0
    )
    field_real = field_real * scale
    field_imag = field_imag * scale
    share_sum = weights[kernel_index] * (field_real * field_real + field_imag * field_imag)
    share_sum = share_sum / total_kernels
    intensity = exchange_sum(share_sum, "kern")
    drive = resist_drive(intensity, target_ext, pixel_active)
    source_real, source_imag = right_stacked(
        drive * field_real, drive * field_imag, col_stack[:field_cols, :], -1.0
    )
    source_real, source_imag = left_stacked(
        row_stack[:, :band], -1.0, source_real, source_imag
    )
    quot_real = source_real * kern_real + source_imag * kern_imag
    quot_imag = source_imag * kern_real - source_real * kern_imag
    back_real, back_imag = apply_left(
        row_cos[margin : margin + band, :],
        row_sin[margin : margin + band, :],
        1.0,
        quot_real,
        quot_imag,
    )
    grad_scale = 2.0 * weights[kernel_index] * scale / total_kernels
    own_cos = col_cos[:, reach : reach + own_cols]
    own_sin = col_sin[:, reach : reach + own_cols]
    own_grad = grad_scale * (product(back_real, own_cos) - product(back_imag, own_sin))
    return exchange_sum(own_grad, "kern")


def solution(mesh):
    return jax.shard_map(
        body,
        mesh=mesh,
        in_specs=(
            P(None, "tile"),
            P("kern", None, None, None),
            P("kern"),
            P(None, "tile"),
            P(None, "tile"),
        ),
        out_specs=P(None, "tile"),
        check_vma=False,
    )
```

```python
import math

import jax
import numpy as np
import jax.numpy as jnp
from jax import lax
from jax.sharding import PartitionSpec as P

BLK = 32


STEEPNESS = 6.0
THRESHOLD = 0.8


def padded(shard, sides, width):
    for axis, dim in sides:
        peers, length = (lax.axis_size(axis), shard.shape[dim])
        up = [(i, (i + 1) % peers) for i in range(peers - 1)]
        down = [(j, i) for i, j in up]
        last = lax.slice_in_dim(shard, length - width, length, axis=dim)
        initial = lax.slice_in_dim(shard, 0, width, axis=dim)
        before = lax.ppermute(last, axis, up)
        after = lax.ppermute(initial, axis, down)
        shard = jnp.concatenate([before, shard, after], axis=dim)
    return shard


def exchange_sum(value, axis):
    peers = lax.axis_size(axis)
    rows, cols = value.shape
    if (rows * cols) % peers:
        return lax.psum(value, axis)
    parts = value.reshape(peers, rows * cols // peers)
    parts = lax.all_to_all(parts, axis, 0, 0, tiled=True)
    total = jnp.sum(parts, axis=0, keepdims=True)
    gathered = lax.all_to_all(jnp.broadcast_to(total, parts.shape), axis, 0, 0, tiled=True)
    return gathered.reshape(rows, cols)


def product(left_mat, right_mat):
    return jnp.dot(
        left_mat, right_mat, precision=lax.Precision.HIGHEST, preferred_element_type=jnp.float32
    )


def twiddle(length):
    series = np.arange(length, dtype=np.int64)
    angle = (series[:, None] * series[None, :] % length) * (2.0 * math.pi / length)
    return (jnp.asarray(np.cos(angle), jnp.float32), jnp.asarray(np.sin(angle), jnp.float32))


def apply_left(cosine, sine, sign, real_part, imag_part):
    width = real_part.shape[1]
    both = jnp.concatenate([real_part, imag_part], axis=1)
    by_cos = product(cosine, both)
    by_sin = product(sine, both)
    return (
        by_cos[:, :width] - sign * by_sin[:, width:],
        by_cos[:, width:] + sign * by_sin[:, :width],
    )


def apply_right(real_part, imag_part, cosine, sine, sign):
    height = real_part.shape[0]
    both = jnp.concatenate([real_part, imag_part], axis=0)
    by_cos = product(both, cosine)
    by_sin = product(both, sine)
    return (
        by_cos[:height] - sign * by_sin[height:],
        by_cos[height:] + sign * by_sin[:height],
    )


def left_stacked(stack, sign, real_part, imag_part):
    height = stack.shape[0] // 2
    width = real_part.shape[1]
    full = product(stack, jnp.concatenate([real_part, imag_part], axis=1))
    return (
        full[:height, :width] - sign * full[height:, width:],
        full[:height, width:] + sign * full[height:, :width],
    )


def right_stacked(real_part, imag_part, stack, sign):
    height = real_part.shape[0]
    width = stack.shape[1] // 2
    full = product(jnp.concatenate([real_part, imag_part], axis=0), stack)
    return (
        full[:height, :width] - sign * full[height:, width:],
        full[height:, :width] + sign * full[:height, width:],
    )


def edge_pixels(frame, margin):
    return jnp.concatenate([frame[:, :margin], frame[:, frame.shape[1] - margin :]], axis=1)


def add_returned(own, returned, margin):
    from_left = returned[:, :margin]
    from_right = returned[:, returned.shape[1] - margin :]
    own = own.at[:, :margin].add(from_left)
    return own.at[:, own.shape[1] - margin :].add(from_right)


def resist_drive(intensity, target_rows, active_rows):
    resist = jax.nn.sigmoid(STEEPNESS * (intensity - THRESHOLD))
    return 2.0 * (resist - target_rows) * active_rows * STEEPNESS * resist * (1.0 - resist)


def body(mask, kernels, weights, target, active):
    band, own_cols = mask.shape
    width = kernels.shape[-1]
    margin = (width - 1) // 2
    reach = 2 * margin
    field_cols = own_cols + reach
    frame_rows = band + 2 * margin
    frame_cols = own_cols + 2 * reach
    total_kernels = kernels.shape[0] * lax.axis_size("kern")
    scale = 1.0 / (frame_rows * frame_cols)
    row_cos, row_sin = twiddle(frame_rows)
    col_cos, col_sin = twiddle(frame_cols)
    row_stack = jnp.concatenate([row_cos, row_sin], axis=0)
    col_stack = jnp.concatenate([col_cos, col_sin], axis=1)
    row_stack, col_stack = lax.optimization_barrier((row_stack, col_stack))
    row_cos, row_sin = row_stack[:frame_rows], row_stack[frame_rows:]
    col_cos, col_sin = col_stack[:, :frame_cols], col_stack[:, frame_cols:]
    block_grid, blocks = active.shape
    block_rows = band // block_grid
    block_cols = own_cols // blocks
    reach_blocks = margin // block_cols
    active_rows = jnp.pad(active.astype(jnp.float32), ((0, 0), (0, own_cols - blocks)))
    extended = padded(mask, (("tile", 1),), reach)
    sides = jnp.concatenate([target.astype(jnp.float32), active_rows], axis=0)
    sides = padded(sides, (("tile", 1),), reach)
    target_ext = sides[:band, margin : margin + field_cols]
    active_row = sides[band:]
    active_ext = jnp.concatenate(
        [
            active_row[:, blocks - reach_blocks : blocks],
            active_row[:, own_cols : own_cols + blocks],
            active_row[:, 2 * own_cols : 2 * own_cols + reach_blocks],
        ],
        axis=1,
    )
    pixel_active = jnp.repeat(jnp.repeat(active_ext, block_rows, axis=0), block_cols, axis=1)
    by_cols = product(extended, col_stack)
    cols_real = by_cols[:, :frame_cols]
    cols_imag = -by_cols[:, frame_cols:]
    spec_real, spec_imag = left_stacked(
        row_stack[:, margin : margin + band], -1.0, cols_real, cols_imag
    )
    kernel_index = 0
    kern_real, kern_imag = left_stacked(
        row_stack[:, :width], 1.0, kernels[kernel_index, 0], kernels[kernel_index, 1]
    )
    kern_real, kern_imag = right_stacked(kern_real, kern_imag, col_stack[:width, :], 1.0)
    prod_real = spec_real * kern_real - spec_imag * kern_imag
    prod_imag = spec_real * kern_imag + spec_imag * kern_real
    field_real, field_imag = apply_left(
        row_cos[:band, :], row_sin[:band, :], 1.0, prod_real, prod_imag
    )
    field_real, field_imag = apply_right(
        field_real, field_imag, col_cos[:, :field_cols], col_sin[:, :field_cols], 1.0
    )
    field_real = field_real * scale
    field_imag = field_imag * scale
    share_sum = weights[kernel_index] * (field_real * field_real + field_imag * field_imag)
    share_sum = share_sum / total_kernels + 0.0 * target_ext
    intensity = exchange_sum(share_sum, "kern")
    drive = resist_drive(intensity, target_ext, pixel_active)
    source_real, source_imag = right_stacked(
        drive * field_real, drive * field_imag, col_stack[:field_cols, :], -1.0
    )
    source_real, source_imag = left_stacked(
        row_stack[:, :band], -1.0, source_real, source_imag
    )
    quot_real = source_real * kern_real + source_imag * kern_imag
    quot_imag = source_imag * kern_real - source_real * kern_imag
    back_real, back_imag = apply_left(
        row_cos[margin : margin + band, :],
        row_sin[margin : margin + band, :],
        1.0,
        quot_real,
        quot_imag,
    )
    grad_scale = 2.0 * weights[kernel_index] * scale / total_kernels
    own_cos = col_cos[:, reach : reach + own_cols]
    own_sin = col_sin[:, reach : reach + own_cols]
    own_grad = grad_scale * (product(back_real, own_cos) - product(back_imag, own_sin))
    return exchange_sum(own_grad, "kern")


def solution(mesh):
    return jax.shard_map(
        body,
        mesh=mesh,
        in_specs=(
            P(None, "tile"),
            P("kern", None, None, None),
            P("kern"),
            P(None, "tile"),
            P(None, "tile"),
        ),
        out_specs=P(None, "tile"),
        check_vma=False,
    )
```

```python
import math

import jax
import numpy as np
import jax.numpy as jnp
from jax import lax
from jax.sharding import PartitionSpec as P

BLK = 32


STEEPNESS = 6.0
THRESHOLD = 0.8


def padded(shard, sides, width):
    for axis, dim in sides:
        peers, length = (lax.axis_size(axis), shard.shape[dim])
        up = [(i, (i + 1) % peers) for i in range(peers - 1)]
        down = [(j, i) for i, j in up]
        last = lax.slice_in_dim(shard, length - width, length, axis=dim)
        initial = lax.slice_in_dim(shard, 0, width, axis=dim)
        before = lax.ppermute(last, axis, up)
        after = lax.ppermute(initial, axis, down)
        shard = jnp.concatenate([before, shard, after], axis=dim)
    return shard


def exchange_sum(value, axis):
    peers = lax.axis_size(axis)
    rows, cols = value.shape
    if (rows * cols) % peers:
        return lax.psum(value, axis)
    parts = value.reshape(peers, rows * cols // peers)
    parts = lax.all_to_all(parts, axis, 0, 0, tiled=True)
    total = jnp.sum(parts, axis=0, keepdims=True)
    gathered = lax.all_to_all(jnp.broadcast_to(total, parts.shape), axis, 0, 0, tiled=True)
    return gathered.reshape(rows, cols)


def product(left_mat, right_mat):
    return jnp.dot(
        left_mat, right_mat, precision=lax.Precision.HIGHEST, preferred_element_type=jnp.float32
    )


def twiddle(length):
    series = np.arange(length, dtype=np.int64)
    angle = (series[:, None] * series[None, :] % length) * (2.0 * math.pi / length)
    return (jnp.asarray(np.cos(angle), jnp.float32), jnp.asarray(np.sin(angle), jnp.float32))


def apply_left(cosine, sine, sign, real_part, imag_part):
    width = real_part.shape[1]
    both = jnp.concatenate([real_part, imag_part], axis=1)
    by_cos = product(cosine, both)
    by_sin = product(sine, both)
    return (
        by_cos[:, :width] - sign * by_sin[:, width:],
        by_cos[:, width:] + sign * by_sin[:, :width],
    )


def apply_right(real_part, imag_part, cosine, sine, sign):
    height = real_part.shape[0]
    both = jnp.concatenate([real_part, imag_part], axis=0)
    by_cos = product(both, cosine)
    by_sin = product(both, sine)
    return (
        by_cos[:height] - sign * by_sin[height:],
        by_cos[height:] + sign * by_sin[:height],
    )


def left_stacked(stack, sign, real_part, imag_part):
    height = stack.shape[0] // 2
    width = real_part.shape[1]
    full = product(stack, jnp.concatenate([real_part, imag_part], axis=1))
    return (
        full[:height, :width] - sign * full[height:, width:],
        full[:height, width:] + sign * full[height:, :width],
    )


def right_stacked(real_part, imag_part, stack, sign):
    height = real_part.shape[0]
    width = stack.shape[1] // 2
    full = product(jnp.concatenate([real_part, imag_part], axis=0), stack)
    return (
        full[:height, :width] - sign * full[height:, width:],
        full[height:, :width] + sign * full[:height, width:],
    )


def edge_pixels(frame, margin):
    return jnp.concatenate([frame[:, :margin], frame[:, frame.shape[1] - margin :]], axis=1)


def add_returned(own, returned, margin):
    from_left = returned[:, :margin]
    from_right = returned[:, returned.shape[1] - margin :]
    own = own.at[:, :margin].add(from_left)
    return own.at[:, own.shape[1] - margin :].add(from_right)


def resist_drive(intensity, target_rows, active_rows):
    resist = jax.nn.sigmoid(STEEPNESS * (intensity - THRESHOLD))
    return 2.0 * (resist - target_rows) * active_rows * STEEPNESS * resist * (1.0 - resist)


def body(mask, kernels, weights, target, active):
    band, own_cols = mask.shape
    width = kernels.shape[-1]
    margin = (width - 1) // 2
    reach = 2 * margin
    field_cols = own_cols + reach
    frame_rows = band + 2 * margin
    frame_cols = own_cols + 2 * reach
    total_kernels = kernels.shape[0] * lax.axis_size("kern")
    scale = 1.0 / (frame_rows * frame_cols)
    row_cos, row_sin = twiddle(frame_rows)
    col_cos, col_sin = twiddle(frame_cols)
    row_stack = jnp.concatenate([row_cos, row_sin], axis=0)
    col_stack = jnp.concatenate([col_cos, col_sin], axis=1)
    row_stack, col_stack = lax.optimization_barrier((row_stack, col_stack))
    row_cos, row_sin = row_stack[:frame_rows], row_stack[frame_rows:]
    col_cos, col_sin = col_stack[:, :frame_cols], col_stack[:, frame_cols:]
    block_grid, blocks = active.shape
    block_rows = band // block_grid
    block_cols = own_cols // blocks
    reach_blocks = margin // block_cols
    active_rows = jnp.pad(active, ((0, 0), (0, own_cols - blocks)))
    whole = jnp.concatenate([target, active_rows], axis=0).astype(jnp.float32)
    stacked = jnp.concatenate([mask, whole], axis=0)
    stacked = padded(stacked, (("tile", 1),), reach)
    extended = stacked[:band]
    target_ext = stacked[band : 2 * band, margin : margin + field_cols]
    active_row = stacked[2 * band :]
    active_ext = jnp.concatenate(
        [
            active_row[:, blocks - reach_blocks : blocks],
            active_row[:, own_cols : own_cols + blocks],
            active_row[:, 2 * own_cols : 2 * own_cols + reach_blocks],
        ],
        axis=1,
    )
    pixel_active = jnp.repeat(jnp.repeat(active_ext, block_rows, axis=0), block_cols, axis=1)
    by_cols = product(extended, col_stack)
    cols_real = by_cols[:, :frame_cols]
    cols_imag = -by_cols[:, frame_cols:]
    spec_real, spec_imag = left_stacked(
        row_stack[:, margin : margin + band], -1.0, cols_real, cols_imag
    )
    kernel_index = 0
    kern_real, kern_imag = left_stacked(
        row_stack[:, :width], 1.0, kernels[kernel_index, 0], kernels[kernel_index, 1]
    )
    kern_real, kern_imag = right_stacked(kern_real, kern_imag, col_stack[:width, :], 1.0)
    prod_real = spec_real * kern_real - spec_imag * kern_imag
    prod_imag = spec_real * kern_imag + spec_imag * kern_real
    field_real, field_imag = apply_left(
        row_cos[:band, :], row_sin[:band, :], 1.0, prod_real, prod_imag
    )
    field_real, field_imag = apply_right(
        field_real, field_imag, col_cos[:, :field_cols], col_sin[:, :field_cols], 1.0
    )
    field_real = field_real * scale
    field_imag = field_imag * scale
    share_sum = weights[kernel_index] * (field_real * field_real + field_imag * field_imag)
    share_sum = share_sum / total_kernels
    intensity = exchange_sum(share_sum, "kern")
    drive = resist_drive(intensity, target_ext, pixel_active)
    source_real, source_imag = right_stacked(
        drive * field_real, drive * field_imag, col_stack[:field_cols, :], -1.0
    )
    source_real, source_imag = left_stacked(
        row_stack[:, :band], -1.0, source_real, source_imag
    )
    quot_real = source_real * kern_real + source_imag * kern_imag
    quot_imag = source_imag * kern_real - source_real * kern_imag
    back_real, back_imag = apply_left(
        row_cos[margin : margin + band, :],
        row_sin[margin : margin + band, :],
        1.0,
        quot_real,
        quot_imag,
    )
    grad_scale = 2.0 * weights[kernel_index] * scale / total_kernels
    own_cos = col_cos[:, reach : reach + own_cols]
    own_sin = col_sin[:, reach : reach + own_cols]
    own_grad = grad_scale * (product(back_real, own_cos) - product(back_imag, own_sin))
    return exchange_sum(own_grad, "kern")


def solution(mesh):
    return jax.shard_map(
        body,
        mesh=mesh,
        in_specs=(
            P(None, "tile"),
            P("kern", None, None, None),
            P("kern"),
            P(None, "tile"),
            P(None, "tile"),
        ),
        out_specs=P(None, "tile"),
        check_vma=False,
    )
```

```python
import math

import jax
import numpy as np
import jax.numpy as jnp
from jax import lax
from jax.sharding import PartitionSpec as P

BLK = 32


STEEPNESS = 6.0
THRESHOLD = 0.8


def padded(shard, sides, width):
    for axis, dim in sides:
        peers, length = (lax.axis_size(axis), shard.shape[dim])
        up = [(i, (i + 1) % peers) for i in range(peers - 1)]
        down = [(j, i) for i, j in up]
        last = lax.slice_in_dim(shard, length - width, length, axis=dim)
        initial = lax.slice_in_dim(shard, 0, width, axis=dim)
        before = lax.ppermute(last, axis, up)
        after = lax.ppermute(initial, axis, down)
        shard = jnp.concatenate([before, shard, after], axis=dim)
    return shard


def exchange_sum(value, axis, spread=False):
    peers = lax.axis_size(axis)
    rows, cols = value.shape
    if (rows * cols) % peers:
        return lax.psum(value, axis)
    parts = value.reshape(peers, rows * cols // peers)
    parts = lax.all_to_all(parts, axis, 0, 0, tiled=True)
    if spread:
        spread_sum = product(jnp.ones((peers, peers), jnp.float32), parts)
    else:
        spread_sum = jnp.broadcast_to(jnp.sum(parts, axis=0, keepdims=True), parts.shape)
    gathered = lax.all_to_all(spread_sum, axis, 0, 0, tiled=True)
    return gathered.reshape(rows, cols)


def product(left_mat, right_mat):
    return jnp.dot(
        left_mat, right_mat, precision=lax.Precision.HIGHEST, preferred_element_type=jnp.float32
    )


def twiddle(length):
    series = np.arange(length, dtype=np.int64)
    angle = (series[:, None] * series[None, :] % length) * (2.0 * math.pi / length)
    return (jnp.asarray(np.cos(angle), jnp.float32), jnp.asarray(np.sin(angle), jnp.float32))


def apply_left(cosine, sine, sign, real_part, imag_part):
    width = real_part.shape[1]
    both = jnp.concatenate([real_part, imag_part], axis=1)
    by_cos = product(cosine, both)
    by_sin = product(sine, both)
    return (
        by_cos[:, :width] - sign * by_sin[:, width:],
        by_cos[:, width:] + sign * by_sin[:, :width],
    )


def apply_right(real_part, imag_part, cosine, sine, sign):
    height = real_part.shape[0]
    both = jnp.concatenate([real_part, imag_part], axis=0)
    by_cos = product(both, cosine)
    by_sin = product(both, sine)
    return (
        by_cos[:height] - sign * by_sin[height:],
        by_cos[height:] + sign * by_sin[:height],
    )


def left_stacked(stack, sign, real_part, imag_part):
    height = stack.shape[0] // 2
    width = real_part.shape[1]
    full = product(stack, jnp.concatenate([real_part, imag_part], axis=1))
    return (
        full[:height, :width] - sign * full[height:, width:],
        full[:height, width:] + sign * full[height:, :width],
    )


def right_stacked(real_part, imag_part, stack, sign):
    height = real_part.shape[0]
    width = stack.shape[1] // 2
    full = product(jnp.concatenate([real_part, imag_part], axis=0), stack)
    return (
        full[:height, :width] - sign * full[height:, width:],
        full[height:, :width] + sign * full[:height, width:],
    )


def edge_pixels(frame, margin):
    return jnp.concatenate([frame[:, :margin], frame[:, frame.shape[1] - margin :]], axis=1)


def add_returned(own, returned, margin):
    from_left = returned[:, :margin]
    from_right = returned[:, returned.shape[1] - margin :]
    own = own.at[:, :margin].add(from_left)
    return own.at[:, own.shape[1] - margin :].add(from_right)


def resist_drive(intensity, target_rows, active_rows):
    resist = jax.nn.sigmoid(STEEPNESS * (intensity - THRESHOLD))
    return 2.0 * (resist - target_rows) * active_rows * STEEPNESS * resist * (1.0 - resist)


def body(mask, kernels, weights, target, active):
    band, own_cols = mask.shape
    width = kernels.shape[-1]
    margin = (width - 1) // 2
    reach = 2 * margin
    field_cols = own_cols + reach
    frame_rows = band + 2 * margin
    frame_cols = own_cols + 2 * reach
    total_kernels = kernels.shape[0] * lax.axis_size("kern")
    scale = 1.0 / (frame_rows * frame_cols)
    row_cos, row_sin = twiddle(frame_rows)
    col_cos, col_sin = twiddle(frame_cols)
    row_stack = jnp.concatenate([row_cos, row_sin], axis=0)
    col_stack = jnp.concatenate([col_cos, col_sin], axis=1)
    row_stack, col_stack = lax.optimization_barrier((row_stack, col_stack))
    row_cos, row_sin = row_stack[:frame_rows], row_stack[frame_rows:]
    col_cos, col_sin = col_stack[:, :frame_cols], col_stack[:, frame_cols:]
    block_grid, blocks = active.shape
    block_rows = band // block_grid
    block_cols = own_cols // blocks
    reach_blocks = margin // block_cols
    active_rows = jnp.pad(active, ((0, 0), (0, own_cols - blocks)))
    whole = jnp.concatenate([target, active_rows], axis=0).astype(jnp.float32)
    stacked = jnp.concatenate([mask, whole], axis=0)
    stacked = padded(stacked, (("tile", 1),), reach)
    extended = stacked[:band]
    target_ext = stacked[band : 2 * band, margin : margin + field_cols]
    active_row = stacked[2 * band :]
    active_ext = jnp.concatenate(
        [
            active_row[:, blocks - reach_blocks : blocks],
            active_row[:, own_cols : own_cols + blocks],
            active_row[:, 2 * own_cols : 2 * own_cols + reach_blocks],
        ],
        axis=1,
    )
    pixel_active = jnp.repeat(jnp.repeat(active_ext, block_rows, axis=0), block_cols, axis=1)
    by_cols = product(extended, col_stack)
    cols_real = by_cols[:, :frame_cols]
    cols_imag = -by_cols[:, frame_cols:]
    spec_real, spec_imag = left_stacked(
        row_stack[:, margin : margin + band], -1.0, cols_real, cols_imag
    )
    kernel_index = 0
    kern_real, kern_imag = left_stacked(
        row_stack[:, :width], 1.0, kernels[kernel_index, 0], kernels[kernel_index, 1]
    )
    kern_real, kern_imag = right_stacked(kern_real, kern_imag, col_stack[:width, :], 1.0)
    prod_real = spec_real * kern_real - spec_imag * kern_imag
    prod_imag = spec_real * kern_imag + spec_imag * kern_real
    field_real, field_imag = apply_left(
        row_cos[:band, :], row_sin[:band, :], 1.0, prod_real, prod_imag
    )
    field_real, field_imag = apply_right(
        field_real, field_imag, col_cos[:, :field_cols], col_sin[:, :field_cols], 1.0
    )
    field_real = field_real * scale
    field_imag = field_imag * scale
    share_sum = weights[kernel_index] * (field_real * field_real + field_imag * field_imag)
    share_sum = share_sum / total_kernels
    intensity = exchange_sum(share_sum, "kern", spread=True)
    drive = resist_drive(intensity, target_ext, pixel_active)
    source_real, source_imag = right_stacked(
        drive * field_real, drive * field_imag, col_stack[:field_cols, :], -1.0
    )
    source_real, source_imag = left_stacked(
        row_stack[:, :band], -1.0, source_real, source_imag
    )
    quot_real = source_real * kern_real + source_imag * kern_imag
    quot_imag = source_imag * kern_real - source_real * kern_imag
    back_real, back_imag = apply_left(
        row_cos[margin : margin + band, :],
        row_sin[margin : margin + band, :],
        1.0,
        quot_real,
        quot_imag,
    )
    grad_scale = 2.0 * weights[kernel_index] * scale / total_kernels
    own_cos = col_cos[:, reach : reach + own_cols]
    own_sin = col_sin[:, reach : reach + own_cols]
    own_grad = grad_scale * (product(back_real, own_cos) - product(back_imag, own_sin))
    return exchange_sum(own_grad, "kern")


def solution(mesh):
    return jax.shard_map(
        body,
        mesh=mesh,
        in_specs=(
            P(None, "tile"),
            P("kern", None, None, None),
            P("kern"),
            P(None, "tile"),
            P(None, "tile"),
        ),
        out_specs=P(None, "tile"),
        check_vma=False,
    )
```

```python
import math

import jax
import numpy as np
import jax.numpy as jnp
from jax import lax
from jax.sharding import PartitionSpec as P

BLK = 32


STEEPNESS = 6.0
THRESHOLD = 0.8


def padded(shard, sides, width):
    for axis, dim in sides:
        peers, length = (lax.axis_size(axis), shard.shape[dim])
        up = [(i, (i + 1) % peers) for i in range(peers - 1)]
        down = [(j, i) for i, j in up]
        last = lax.slice_in_dim(shard, length - width, length, axis=dim)
        initial = lax.slice_in_dim(shard, 0, width, axis=dim)
        before = lax.ppermute(last, axis, up)
        after = lax.ppermute(initial, axis, down)
        shard = jnp.concatenate([before, shard, after], axis=dim)
    return shard


def exchange_sum(value, axis, spread=False):
    peers = lax.axis_size(axis)
    rows, cols = value.shape
    if (rows * cols) % peers:
        return lax.psum(value, axis)
    parts = value.reshape(peers, rows * cols // peers)
    parts = lax.all_to_all(parts, axis, 0, 0, tiled=True)
    if spread:
        spread_sum = product(jnp.ones((peers, peers), jnp.float32), parts)
    else:
        spread_sum = jnp.broadcast_to(jnp.sum(parts, axis=0, keepdims=True), parts.shape)
    gathered = lax.all_to_all(spread_sum, axis, 0, 0, tiled=True)
    return gathered.reshape(rows, cols)


def product(left_mat, right_mat):
    return jnp.dot(
        left_mat, right_mat, precision=lax.Precision.HIGHEST, preferred_element_type=jnp.float32
    )


def twiddle(length):
    series = np.arange(length, dtype=np.int64)
    angle = (series[:, None] * series[None, :] % length) * (2.0 * math.pi / length)
    return (jnp.asarray(np.cos(angle), jnp.float32), jnp.asarray(np.sin(angle), jnp.float32))


def apply_left(cosine, sine, sign, real_part, imag_part):
    width = real_part.shape[1]
    both = jnp.concatenate([real_part, imag_part], axis=1)
    by_cos = product(cosine, both)
    by_sin = product(sine, both)
    return (
        by_cos[:, :width] - sign * by_sin[:, width:],
        by_cos[:, width:] + sign * by_sin[:, :width],
    )


def apply_right(real_part, imag_part, cosine, sine, sign):
    height = real_part.shape[0]
    both = jnp.concatenate([real_part, imag_part], axis=0)
    by_cos = product(both, cosine)
    by_sin = product(both, sine)
    return (
        by_cos[:height] - sign * by_sin[height:],
        by_cos[height:] + sign * by_sin[:height],
    )


def left_stacked(stack, sign, real_part, imag_part):
    height = stack.shape[0] // 2
    width = real_part.shape[1]
    full = product(stack, jnp.concatenate([real_part, imag_part], axis=1))
    return (
        full[:height, :width] - sign * full[height:, width:],
        full[:height, width:] + sign * full[height:, :width],
    )


def right_stacked(real_part, imag_part, stack, sign):
    height = real_part.shape[0]
    width = stack.shape[1] // 2
    full = product(jnp.concatenate([real_part, imag_part], axis=0), stack)
    return (
        full[:height, :width] - sign * full[height:, width:],
        full[height:, :width] + sign * full[:height, width:],
    )


def edge_pixels(frame, margin):
    return jnp.concatenate([frame[:, :margin], frame[:, frame.shape[1] - margin :]], axis=1)


def add_returned(own, returned, margin):
    from_left = returned[:, :margin]
    from_right = returned[:, returned.shape[1] - margin :]
    own = own.at[:, :margin].add(from_left)
    return own.at[:, own.shape[1] - margin :].add(from_right)


def resist_drive(intensity, target_rows, active_rows):
    resist = jax.nn.sigmoid(STEEPNESS * (intensity - THRESHOLD))
    return 2.0 * (resist - target_rows) * active_rows * STEEPNESS * resist * (1.0 - resist)


def body(mask, kernels, weights, target, active):
    band, own_cols = mask.shape
    width = kernels.shape[-1]
    margin = (width - 1) // 2
    reach = 2 * margin
    field_cols = own_cols + reach
    frame_rows = band + 2 * margin
    frame_cols = own_cols + 2 * reach
    total_kernels = kernels.shape[0] * lax.axis_size("kern")
    scale = 1.0 / (frame_rows * frame_cols)
    row_cos, row_sin = twiddle(frame_rows)
    col_cos, col_sin = twiddle(frame_cols)
    row_stack = jnp.concatenate([row_cos, row_sin], axis=0)
    col_stack = jnp.concatenate([col_cos, col_sin], axis=1)
    field_rows = jnp.concatenate([row_cos[:band], row_sin[:band]], axis=0)
    back_rows = jnp.concatenate(
        [row_cos[margin : margin + band], row_sin[margin : margin + band]], axis=0
    )
    row_stack, col_stack, field_rows, back_rows = lax.optimization_barrier(
        (row_stack, col_stack, field_rows, back_rows)
    )
    row_cos, row_sin = row_stack[:frame_rows], row_stack[frame_rows:]
    col_cos, col_sin = col_stack[:, :frame_cols], col_stack[:, frame_cols:]
    block_grid, blocks = active.shape
    block_rows = band // block_grid
    block_cols = own_cols // blocks
    reach_blocks = margin // block_cols
    active_rows = jnp.pad(active, ((0, 0), (0, own_cols - blocks)))
    whole = jnp.concatenate([target, active_rows], axis=0).astype(jnp.float32)
    stacked = jnp.concatenate([mask, whole], axis=0)
    stacked = padded(stacked, (("tile", 1),), reach)
    extended = stacked[:band]
    target_ext = stacked[band : 2 * band, margin : margin + field_cols]
    active_row = stacked[2 * band :]
    active_ext = jnp.concatenate(
        [
            active_row[:, blocks - reach_blocks : blocks],
            active_row[:, own_cols : own_cols + blocks],
            active_row[:, 2 * own_cols : 2 * own_cols + reach_blocks],
        ],
        axis=1,
    )
    pixel_active = jnp.repeat(jnp.repeat(active_ext, block_rows, axis=0), block_cols, axis=1)
    by_cols = product(extended, col_stack)
    cols_real = by_cols[:, :frame_cols]
    cols_imag = -by_cols[:, frame_cols:]
    spec_real, spec_imag = left_stacked(
        row_stack[:, margin : margin + band], -1.0, cols_real, cols_imag
    )
    kernel_index = 0
    kern_real, kern_imag = left_stacked(
        row_stack[:, :width], 1.0, kernels[kernel_index, 0], kernels[kernel_index, 1]
    )
    kern_real, kern_imag = right_stacked(kern_real, kern_imag, col_stack[:width, :], 1.0)
    prod_real = spec_real * kern_real - spec_imag * kern_imag
    prod_imag = spec_real * kern_imag + spec_imag * kern_real
    field_real, field_imag = left_stacked(field_rows, 1.0, prod_real, prod_imag)
    field_real, field_imag = apply_right(
        field_real, field_imag, col_cos[:, :field_cols], col_sin[:, :field_cols], 1.0
    )
    field_real = field_real * scale
    field_imag = field_imag * scale
    share_sum = weights[kernel_index] * (field_real * field_real + field_imag * field_imag)
    share_sum = share_sum / total_kernels
    intensity = exchange_sum(share_sum, "kern", spread=True)
    drive = resist_drive(intensity, target_ext, pixel_active)
    source_real, source_imag = right_stacked(
        drive * field_real, drive * field_imag, col_stack[:field_cols, :], -1.0
    )
    source_real, source_imag = left_stacked(
        row_stack[:, :band], -1.0, source_real, source_imag
    )
    quot_real = source_real * kern_real + source_imag * kern_imag
    quot_imag = source_imag * kern_real - source_real * kern_imag
    back_real, back_imag = left_stacked(back_rows, 1.0, quot_real, quot_imag)
    grad_scale = 2.0 * weights[kernel_index] * scale / total_kernels
    own_cos = col_cos[:, reach : reach + own_cols]
    own_sin = col_sin[:, reach : reach + own_cols]
    own_grad = grad_scale * (product(back_real, own_cos) - product(back_imag, own_sin))
    return exchange_sum(own_grad, "kern")


def solution(mesh):
    return jax.shard_map(
        body,
        mesh=mesh,
        in_specs=(
            P(None, "tile"),
            P("kern", None, None, None),
            P("kern"),
            P(None, "tile"),
            P(None, "tile"),
        ),
        out_specs=P(None, "tile"),
        check_vma=False,
    )
```
